1024 devices in a mesh: lat: 32 (over y, x, core), lev: 32 (over z).
Axes of the slice: x: 4, y: 4, z: 32, core: 2. Of those that a mesh axis runs over, the one named last changes fastest.
Arguments:
- tracers: float32 [3, 64, 256, 2880], P(None, 'lev', 'lat'), may hold values from -6 to 6
- courant_x: float32 [64, 256, 2880], P('lev', 'lat'), may hold values from -0.8 to 0.8
- courant_y: float32 [64, 256, 2880], P('lev', 'lat'), may hold values from -0.8 to 0.8
- thickness: float32 [256, 2880, 64], P('lat', 'lev'), may hold values from 0.5 to 5
- targets: int32 [256, 2880, 64], P('lat', 'lev'), may hold values from 0 to 31, never falling along the last dimension, each value on 1 to 4 neighbouring positions
Outputs:
- remapped: float32 [3, 32, 256, 2880], P(None, 'lev', 'lat')
The draws below stay inside these ranges and needn't reach their ends.
Inputs may be any that keep to these rules, and one draw needn't show every extreme that they name: Along the levels of each column the targets never fall; each of the 32 new levels receives 1 to 4 source levels, and in each column one receives exactly 4.
All inputs are finite; a program needn't handle non-finite values.
Results may differ from the reference program's by a relative error of at most 0.0003.
Values sent between devices are 32-bit elements; how exact they have to be, the bound alone decides.
No kernel may reach another device: no remote copies, remote signals or barrier semaphores. Data moves between devices by JAX's collectives and lax.ppermute only.
A program may use at most 64 MiB of HBM per device.

```python
import math
import jax
import jax.numpy as jnp
import numpy as np
from jax import lax

NLON = 2880
TRACERS = 3
SUBSTEPS = 2
MOST = 4
LAT = 256
LEV = 64
LEV_OUT = 32


def block_scale(key, dims, shards, least, high):
    level, own = 1.0, jax.random.fold_in(key, 6)
    for position, blocks in shards:
        draws = jnp.exp(jax.random.uniform(jax.random.fold_in(own, position), (blocks,), jnp.float32, least / len(shards), high / len(shards)))
        level = level * jnp.repeat(draws, dims[position] // blocks).reshape([-1 if axis == position else 1 for axis in range(len(dims))])
    return level


def length_profile(number_of, total, limit, skew):
    portions = [(1 << 20) // math.isqrt(grade ** skew) + 1 for grade in range(2, number_of + 1)]
    spare, given = total - limit - (number_of - 1), [1] * (number_of - 1)
    while spare > 0:
        movable = [i for i in range(number_of - 1) if given[i] < limit]
        mass, remaining = sum([portions[i] for i in movable]), spare
        for i in movable:
            extra = min(limit - given[i], max(1, remaining * portions[i] // mass), spare)
            given[i] = given[i] + extra
            spare = spare - extra
    return np.array([limit] + given)


def uneven(key, count, total, reach, skew):
    if count == 2:
        one = jax.random.randint(key, (), max(1, total - reach), min(reach, total - 1) + 1)
        return jnp.stack([one, total - one])
    lengths = jnp.asarray(length_profile(count, total, reach, skew), jnp.int32)
    twos = (count - 1) // 2
    giver, sink = lengths[1:1 + 2 * twos:2], lengths[2:2 + 2 * twos:2]
    room = jnp.minimum(giver - 1, reach - sink)
    moved = jax.random.randint(jax.random.fold_in(key, 1), (twos,), 0, 1 << 20) % (room + 1)
    lengths = lengths.at[1:1 + 2 * twos:2].set(giver - moved).at[2:2 + 2 * twos:2].set(sink + moved)
    return lengths[jax.random.permutation(jax.random.fold_in(key, 2), count)]


def centred(rng, dims, scale, reach, shards=(), held_as=jnp.bfloat16):
    array = scale * jax.random.normal(rng, dims, jnp.float32)
    if shards:
        array = array * block_scale(rng, dims, shards, -0.22, 0.18)
    return jnp.clip(array, -reach, reach).astype(held_as)


def setup_inputs(seed: int = 0) -> dict:
    key_of = jax.random.split(jax.random.key(seed), 6)
    tracers = centred(key_of[0], (TRACERS, LEV, LAT, NLON), 1.0, 6.0, ((1, 32), (2, 32)), jnp.float32)
    courant_x = jnp.clip(jax.random.uniform(key_of[1], (LEV, LAT, NLON), jnp.float32, -0.8, 0.8) * block_scale(key_of[1], (LEV, LAT, NLON), ((0, 32), (1, 32)), -0.4, 0.0), -0.8, 0.8)
    courant_y = jnp.clip(jax.random.uniform(key_of[2], (LEV, LAT, NLON), jnp.float32, -0.8, 0.8) * block_scale(key_of[2], (LEV, LAT, NLON), ((0, 32), (1, 32)), -0.4, 0.0), -0.8, 0.8)
    thickness = jnp.clip(jnp.exp(math.log(5.0) - 2.3025851 * jax.random.uniform(key_of[3], (LAT, NLON, LEV), jnp.float32) ** block_scale(key_of[3], (LAT, NLON, LEV), ((0, 32), (1, 32)), -0.2, 0.2)), 0.5, 5.0)
    targets = jax.vmap(lambda own: jnp.searchsorted(jnp.cumsum(uneven(own, LEV_OUT, LEV, MOST, 0)), jnp.arange(LEV), side="right"))(jax.random.split(key_of[4], LAT * NLON)).reshape((LAT, NLON, LEV)).astype(jnp.int32)
    return {"tracers": tracers, "courant_x": courant_x, "courant_y": courant_y, "thickness": thickness, "targets": targets}


def ppm_sweep(padded, faces, axis, count):
    def piece(start, stop):
        return lax.slice_in_dim(padded, start, stop, axis=axis)

    face_val = (7.0 / 12.0) * (piece(1, count + 4) + piece(2, count + 5)) - (1.0 / 12.0) * (piece(0, count + 3) + piece(3, count + 6))
    cell_midpoint = piece(2, count + 4)
    left_face = lax.slice_in_dim(face_val, 0, count + 2, axis=axis)
    right_face = lax.slice_in_dim(face_val, 1, count + 3, axis=axis)
    slope = right_face - left_face
    curve = 6.0 * (cell_midpoint - 0.5 * (left_face + right_face))

    def lower(x):
        return lax.slice_in_dim(x, 0, count + 1, axis=axis)

    def upper(x):
        return lax.slice_in_dim(x, 1, count + 2, axis=axis)

    from_left = lower(right_face) - 0.5 * faces * (lower(slope) - (1.0 - 2.0 * faces / 3.0) * lower(curve))
    from_right = upper(left_face) - 0.5 * faces * (upper(slope) + (1.0 + 2.0 * faces / 3.0) * upper(curve))
    flux = faces * jnp.where(faces > 0, from_left, from_right)
    inner = piece(3, count + 3)
    return inner - (lax.slice_in_dim(flux, 1, count + 1, axis=axis) - lax.slice_in_dim(flux, 0, count, axis=axis))


def lon_sweep(field, courant_x):
    count = field.shape[-1]
    padded = jnp.concatenate([field[..., -3:], field, field[..., :3]], axis=-1)
    faces = jnp.concatenate([courant_x[..., -1:], courant_x], axis=-1)
    return ppm_sweep(padded, faces, field.ndim - 1, count)


def lat_sweep(field, courant_y):
    count = field.shape[1]
    empty_row_block = jnp.zeros((field.shape[0], 3, field.shape[2]), jnp.float32)
    padded = jnp.concatenate([empty_row_block, field, empty_row_block], axis=1)
    edge = jnp.zeros((field.shape[0], 1, field.shape[2]), jnp.float32)
    faces = jnp.concatenate([edge, courant_y[:, :-1], edge], axis=1)
    return ppm_sweep(padded, faces, 1, count)


def reference(tracers, courant_x, courant_y, thickness, targets):
    def transport_tracer(field):
        for step in range(SUBSTEPS):
            field = lon_sweep(field, courant_x)
            field = lat_sweep(field, courant_y)
        return field

    advected = lax.map(transport_tracer, tracers)
    levels = jnp.arange(LEV_OUT, dtype=jnp.int32)

    def remap_row(inputs):
        row_tracers, row_layer_thickness, row_targets = inputs
        indicator_matrix = (row_targets[:, :, None] == levels[None, None, :]).astype(jnp.float32)
        layer_mass = row_tracers * jnp.transpose(row_layer_thickness)[None]
        target_layer_mass = jnp.einsum("mia,gim->gam", indicator_matrix, layer_mass, precision=lax.Precision.HIGHEST)
        target_layer_thickness = jnp.einsum("nwi,nw->in", indicator_matrix, row_layer_thickness, precision=lax.Precision.HIGHEST)
        return target_layer_mass / target_layer_thickness[None]

    rows_out = lax.map(remap_row, (jnp.transpose(advected, (2, 0, 1, 3)), thickness, targets))
    return jnp.transpose(rows_out, (1, 2, 0, 3))
```

```python
import jax
import jax.numpy as jnp
from jax import lax
from jax.sharding import PartitionSpec as P

SUBSTEPS = 2


def padded_2(cells, sides, width):
    for axis, dim in sides:
        count = lax.axis_size(axis)
        ends = count - 1
        head = lax.slice_in_dim(cells, 0, width, axis=dim)
        tail = lax.slice_in_dim(cells, cells.shape[dim] - width, cells.shape[dim], axis=dim)
        cells = jnp.concatenate(
            [
                lax.ppermute(tail, axis, [(i, (i + 1) % count) for i in range(ends)]),
                cells,
                lax.ppermute(head, axis, [((i + 1) % count, i) for i in range(ends)]),
            ],
            axis=dim,
        )
    return cells


def ppm_sweep(padded, faces, axis, count):

    def piece(start, stop):
        return lax.slice_in_dim(padded, start, stop, axis=axis)

    face_val = 7.0 / 12.0 * (piece(1, count + 4) + piece(2, count + 5)) - 1.0 / 12.0 * (
        piece(0, count + 3) + piece(3, count + 6)
    )
    cell_midpoint = piece(2, count + 4)
    left_face = lax.slice_in_dim(face_val, 0, count + 2, axis=axis)
    right_face = lax.slice_in_dim(face_val, 1, count + 3, axis=axis)
    slope = right_face - left_face
    curve = 6.0 * (cell_midpoint - 0.5 * (left_face + right_face))

    def lower(x):
        return lax.slice_in_dim(x, 0, count + 1, axis=axis)

    def upper(x):
        return lax.slice_in_dim(x, 1, count + 2, axis=axis)

    from_left = lower(right_face) - 0.5 * faces * (
        lower(slope) - (1.0 - 2.0 * faces / 3.0) * lower(curve)
    )
    from_right = upper(left_face) - 0.5 * faces * (
        upper(slope) + (1.0 + 2.0 * faces / 3.0) * upper(curve)
    )
    flux = faces * jnp.where(faces > 0, from_left, from_right)
    inner = piece(3, count + 3)
    return inner - (
        lax.slice_in_dim(flux, 1, count + 1, axis=axis)
        - lax.slice_in_dim(flux, 0, count, axis=axis)
    )


def lon_sweep(field, courant_x):
    count = field.shape[-1]
    padded = jnp.concatenate([field[..., -3:], field, field[..., :3]], axis=-1)
    faces = jnp.concatenate([courant_x[..., -1:], courant_x], axis=-1)
    return ppm_sweep(padded, faces, 3, count)


def lat_sweep(padded, faces, first_row, total_rows):
    count = padded.shape[2] - 6
    face_rows = first_row - 1 + jnp.arange(count + 1, dtype=jnp.int32)
    valid = ((face_rows >= 0) & (face_rows <= total_rows - 2)).astype(jnp.float32)
    faces = faces * valid[None, :, None]
    swept = ppm_sweep(padded, faces, 2, count)
    cell_rows = first_row + jnp.arange(count, dtype=jnp.int32)
    inside = ((cell_rows >= 0) & (cell_rows < total_rows)).astype(jnp.float32)
    return swept * inside[None, None, :, None]


def remap_columns(adv, thick, tg, levels_out):
    ks = jnp.arange(levels_out, dtype=jnp.int32)
    member = tg[None] == ks[:, None, None, None]
    mass = adv * thick[None]
    new_mass = jnp.sum(jnp.where(member[None], mass[:, None], 0.0), axis=2)
    new_thick = jnp.sum(jnp.where(member, thick[None], 0.0), axis=1)
    return jnp.transpose(new_mass / new_thick[None], (1, 0, 2, 3))


def local(tracers, courant_x, courant_y, thickness, targets):
    rows = tracers.shape[2]
    kinds = tracers.shape[0]
    total_rows = rows * lax.axis_size("lat")
    first_row = lax.axis_index("lat") * rows
    parts = lax.axis_size("lev")
    lon = tracers.shape[3]
    width = lon // parts
    levels_out = tracers.shape[1] * parts // 2
    field = tracers
    for step in range(SUBSTEPS):
        field = lon_sweep(field, courant_x)
        stacked = jnp.concatenate([field, courant_y[None]], axis=0)
        padded = padded_2(stacked, (("lat", 2),), 3)
        field = lat_sweep(padded[:kinds], padded[kinds][:, 2 : rows + 3], first_row, total_rows)
    blocks = jnp.stack([field[..., c * width : (c + 1) * width] for c in range(parts)], axis=0)
    got = lax.all_to_all(blocks, "lev", split_axis=0, concat_axis=0, tiled=True)
    adv = jnp.transpose(got, (1, 0, 2, 3, 4)).reshape(kinds, -1, rows, width)
    thick = jnp.transpose(thickness, (2, 0, 1))
    tg = jnp.transpose(targets, (2, 0, 1))
    out = remap_columns(adv, thick, tg, levels_out)
    back = lax.all_to_all(out, "lev", split_axis=0, concat_axis=0, tiled=True)
    return jnp.concatenate([back[c] for c in range(parts)], axis=-1)[:, None]


def solution(mesh):
    placed = (
        P(None, "lev", "lat", None),
        P("lev", "lat", None),
        P("lev", "lat", None),
        P("lat", "lev", None),
        P("lat", "lev", None),
    )
    return jax.shard_map(
        local, mesh=mesh, in_specs=placed, out_specs=P(None, "lev", "lat", None), check_vma=False
    )
```

```python
import jax
import jax.numpy as jnp
from jax import lax
from jax.sharding import PartitionSpec as P

SUBSTEPS = 2


def padded_2(cells, sides, width):
    for axis, dim in sides:
        count = lax.axis_size(axis)
        ends = count - 1
        head = lax.slice_in_dim(cells, 0, width, axis=dim)
        tail = lax.slice_in_dim(cells, cells.shape[dim] - width, cells.shape[dim], axis=dim)
        cells = jnp.concatenate(
            [
                lax.ppermute(tail, axis, [(i, (i + 1) % count) for i in range(ends)]),
                cells,
                lax.ppermute(head, axis, [((i + 1) % count, i) for i in range(ends)]),
            ],
            axis=dim,
        )
    return cells


def ppm_sweep(padded, faces, axis, count):

    def piece(start, stop):
        return lax.slice_in_dim(padded, start, stop, axis=axis)

    face_val = 7.0 / 12.0 * (piece(1, count + 4) + piece(2, count + 5)) - 1.0 / 12.0 * (
        piece(0, count + 3) + piece(3, count + 6)
    )
    cell_midpoint = piece(2, count + 4)
    left_face = lax.slice_in_dim(face_val, 0, count + 2, axis=axis)
    right_face = lax.slice_in_dim(face_val, 1, count + 3, axis=axis)
    slope = right_face - left_face
    curve = 6.0 * (cell_midpoint - 0.5 * (left_face + right_face))

    def lower(x):
        return lax.slice_in_dim(x, 0, count + 1, axis=axis)

    def upper(x):
        return lax.slice_in_dim(x, 1, count + 2, axis=axis)

    from_left = lower(right_face) - 0.5 * faces * (
        lower(slope) - (1.0 - 2.0 * faces / 3.0) * lower(curve)
    )
    from_right = upper(left_face) - 0.5 * faces * (
        upper(slope) + (1.0 + 2.0 * faces / 3.0) * upper(curve)
    )
    flux = faces * jnp.where(faces > 0, from_left, from_right)
    inner = piece(3, count + 3)
    return inner - (
        lax.slice_in_dim(flux, 1, count + 1, axis=axis)
        - lax.slice_in_dim(flux, 0, count, axis=axis)
    )


def lon_sweep(field, courant_x):
    count = field.shape[-1]
    padded = jnp.concatenate([field[..., -3:], field, field[..., :3]], axis=-1)
    faces = jnp.concatenate([courant_x[..., -1:], courant_x], axis=-1)
    return ppm_sweep(padded, faces, 3, count)


def lat_sweep(padded, faces, first_row, total_rows):
    count = padded.shape[2] - 6
    face_rows = first_row - 1 + jnp.arange(count + 1, dtype=jnp.int32)
    valid = ((face_rows >= 0) & (face_rows <= total_rows - 2)).astype(jnp.float32)
    faces = faces * valid[None, :, None]
    swept = ppm_sweep(padded, faces, 2, count)
    cell_rows = first_row + jnp.arange(count, dtype=jnp.int32)
    inside = ((cell_rows >= 0) & (cell_rows < total_rows)).astype(jnp.float32)
    return swept * inside[None, None, :, None]


def remap_columns(adv, thick, tg, levels_out):
    ks = jnp.arange(levels_out, dtype=jnp.int32)
    member = tg[None] == ks[:, None, None, None]
    mass = adv * thick[None]
    new_mass = jnp.sum(jnp.where(member[None], mass[:, None], 0.0), axis=2)
    new_thick = jnp.sum(jnp.where(member, thick[None], 0.0), axis=1)
    return jnp.transpose(new_mass / new_thick[None], (1, 0, 2, 3))


def local(tracers, courant_x, courant_y, thickness, targets):
    rows = tracers.shape[2]
    kinds = tracers.shape[0]
    total_rows = rows * lax.axis_size("lat")
    first_row = lax.axis_index("lat") * rows
    parts = lax.axis_size("lev")
    lon = tracers.shape[3]
    width = lon // parts
    levels_out = tracers.shape[1] * parts // 2
    field = tracers
    for step in range(SUBSTEPS):
        field = lon_sweep(field, courant_x)
        stacked = jnp.concatenate([field, courant_y[None]], axis=0)
        padded = padded_2(stacked, (("lat", 2),), 3)
        field = lat_sweep(padded[:kinds], padded[kinds][:, 2 : rows + 3], first_row, total_rows)
    blocks = jnp.stack([field[..., c * width : (c + 1) * width] for c in range(parts)], axis=0)
    got = lax.all_to_all(blocks.reshape(parts, -1), "lev", split_axis=0, concat_axis=0, tiled=True).reshape(blocks.shape)
    adv = jnp.transpose(got, (1, 0, 2, 3, 4)).reshape(kinds, -1, rows, width)
    thick = jnp.transpose(thickness, (2, 0, 1))
    tg = jnp.transpose(targets, (2, 0, 1))
    out = remap_columns(adv, thick, tg, levels_out)
    back = lax.all_to_all(out.reshape(parts, -1), "lev", split_axis=0, concat_axis=0, tiled=True).reshape(out.shape)
    return jnp.concatenate([back[c] for c in range(parts)], axis=-1)[:, None]


def solution(mesh):
    placed = (
        P(None, "lev", "lat", None),
        P("lev", "lat", None),
        P("lev", "lat", None),
        P("lat", "lev", None),
        P("lat", "lev", None),
    )
    return jax.shard_map(
        local, mesh=mesh, in_specs=placed, out_specs=P(None, "lev", "lat", None), check_vma=False
    )
```

```python
import jax
import jax.numpy as jnp
from jax import lax
from jax.sharding import PartitionSpec as P
from jax.experimental import pallas as pl
from jax.experimental.pallas import tpu as pltpu

SUBSTEPS = 2


def padded_2(cells, sides, width):
    for axis, dim in sides:
        count = lax.axis_size(axis)
        ends = count - 1
        head = lax.slice_in_dim(cells, 0, width, axis=dim)
        tail = lax.slice_in_dim(cells, cells.shape[dim] - width, cells.shape[dim], axis=dim)
        cells = jnp.concatenate(
            [
                lax.ppermute(tail, axis, [(i, (i + 1) % count) for i in range(ends)]),
                cells,
                lax.ppermute(head, axis, [((i + 1) % count, i) for i in range(ends)]),
            ],
            axis=dim,
        )
    return cells


def ppm_sweep(padded, faces, axis, count):

    def piece(start, stop):
        return lax.slice_in_dim(padded, start, stop, axis=axis)

    face_val = 7.0 / 12.0 * (piece(1, count + 4) + piece(2, count + 5)) - 1.0 / 12.0 * (
        piece(0, count + 3) + piece(3, count + 6)
    )
    cell_midpoint = piece(2, count + 4)
    left_face = lax.slice_in_dim(face_val, 0, count + 2, axis=axis)
    right_face = lax.slice_in_dim(face_val, 1, count + 3, axis=axis)
    slope = right_face - left_face
    curve = 6.0 * (cell_midpoint - 0.5 * (left_face + right_face))

    def lower(x):
        return lax.slice_in_dim(x, 0, count + 1, axis=axis)

    def upper(x):
        return lax.slice_in_dim(x, 1, count + 2, axis=axis)

    from_left = lower(right_face) - 0.5 * faces * (
        lower(slope) - (1.0 - 2.0 * faces / 3.0) * lower(curve)
    )
    from_right = upper(left_face) - 0.5 * faces * (
        upper(slope) + (1.0 + 2.0 * faces / 3.0) * upper(curve)
    )
    flux = faces * jnp.where(faces > 0, from_left, from_right)
    inner = piece(3, count + 3)
    return inner - (
        lax.slice_in_dim(flux, 1, count + 1, axis=axis)
        - lax.slice_in_dim(flux, 0, count, axis=axis)
    )


def lon_kernel(padded_ref, faces_ref, out_ref):
    count = out_ref.shape[-1]
    out_ref[...] = ppm_sweep(padded_ref[...], faces_ref[...][None], 3, count)


def lon_sweep(field, courant_x):
    count = field.shape[-1]
    padded = jnp.concatenate([field[..., -3:], field, field[..., :3]], axis=-1)
    faces = jnp.concatenate([courant_x[..., -1:], courant_x], axis=-1)
    return pl.pallas_call(
        lon_kernel,
        out_shape=jax.ShapeDtypeStruct(field.shape, field.dtype),
    )(padded, faces)


def lat_kernel(padded_ref, faces_ref, inside_ref, out_ref):
    count = out_ref.shape[2]
    swept = ppm_sweep(padded_ref[...], faces_ref[...][None], 2, count)
    out_ref[...] = swept * inside_ref[...][None, None]


def lat_sweep(padded, faces, first_row, total_rows):
    count = padded.shape[2] - 6
    face_rows = first_row - 1 + jnp.arange(count + 1, dtype=jnp.int32)
    valid = ((face_rows >= 0) & (face_rows <= total_rows - 2)).astype(jnp.float32)
    faces = faces * valid[None, :, None]
    cell_rows = first_row + jnp.arange(count, dtype=jnp.int32)
    inside = ((cell_rows >= 0) & (cell_rows < total_rows)).astype(jnp.float32)
    shape = padded.shape[:2] + (count, padded.shape[3])
    return pl.pallas_call(
        lat_kernel,
        out_shape=jax.ShapeDtypeStruct(shape, padded.dtype),
    )(padded, faces, inside[:, None])


def remap_columns(adv, thick, tg, levels_out):
    ks = jnp.arange(levels_out, dtype=jnp.int32)
    member = tg[None] == ks[:, None, None, None]
    mass = adv * thick[None]
    new_mass = jnp.sum(jnp.where(member[None], mass[:, None], 0.0), axis=2)
    new_thick = jnp.sum(jnp.where(member, thick[None], 0.0), axis=1)
    return jnp.transpose(new_mass / new_thick[None], (1, 0, 2, 3))


def local(tracers, courant_x, courant_y, thickness, targets):
    rows = tracers.shape[2]
    kinds = tracers.shape[0]
    total_rows = rows * lax.axis_size("lat")
    first_row = lax.axis_index("lat") * rows
    parts = lax.axis_size("lev")
    lon = tracers.shape[3]
    width = lon // parts
    levels_out = tracers.shape[1] * parts // 2
    field = tracers
    for step in range(SUBSTEPS):
        field = lon_sweep(field, courant_x)
        stacked = jnp.concatenate([field, courant_y[None]], axis=0)
        padded = padded_2(stacked, (("lat", 2),), 3)
        field = lat_sweep(padded[:kinds], padded[kinds][:, 2 : rows + 3], first_row, total_rows)
    blocks = jnp.stack([field[..., c * width : (c + 1) * width] for c in range(parts)], axis=0)
    got = lax.all_to_all(blocks.reshape(parts, -1), "lev", split_axis=0, concat_axis=0, tiled=True).reshape(blocks.shape)
    adv = jnp.transpose(got, (1, 0, 2, 3, 4)).reshape(kinds, -1, rows, width)
    thick = jnp.transpose(thickness, (2, 0, 1))
    tg = jnp.transpose(targets, (2, 0, 1))
    out = remap_columns(adv, thick, tg, levels_out)
    back = lax.all_to_all(out.reshape(parts, -1), "lev", split_axis=0, concat_axis=0, tiled=True).reshape(out.shape)
    return jnp.concatenate([back[c] for c in range(parts)], axis=-1)[:, None]


def solution(mesh):
    placed = (
        P(None, "lev", "lat", None),
        P("lev", "lat", None),
        P("lev", "lat", None),
        P("lat", "lev", None),
        P("lat", "lev", None),
    )
    return jax.shard_map(
        local, mesh=mesh, in_specs=placed, out_specs=P(None, "lev", "lat", None), check_vma=False
    )
```

```python
import jax
import jax.numpy as jnp
from jax import lax
from jax.sharding import PartitionSpec as P

SUBSTEPS = 2


def padded_2(cells, sides, width):
    for axis, dim in sides:
        count = lax.axis_size(axis)
        ends = count - 1
        head = lax.slice_in_dim(cells, 0, width, axis=dim)
        tail = lax.slice_in_dim(cells, cells.shape[dim] - width, cells.shape[dim], axis=dim)
        cells = jnp.concatenate(
            [
                lax.ppermute(tail, axis, [(i, (i + 1) % count) for i in range(ends)]),
                cells,
                lax.ppermute(head, axis, [((i + 1) % count, i) for i in range(ends)]),
            ],
            axis=dim,
        )
    return cells


def ppm_sweep(padded, faces, axis, count):

    def piece(start, stop):
        return lax.slice_in_dim(padded, start, stop, axis=axis)

    face_val = 7.0 / 12.0 * (piece(1, count + 4) + piece(2, count + 5)) - 1.0 / 12.0 * (
        piece(0, count + 3) + piece(3, count + 6)
    )
    cell_midpoint = piece(2, count + 4)
    left_face = lax.slice_in_dim(face_val, 0, count + 2, axis=axis)
    right_face = lax.slice_in_dim(face_val, 1, count + 3, axis=axis)
    slope = right_face - left_face
    curve = 6.0 * (cell_midpoint - 0.5 * (left_face + right_face))

    def lower(x):
        return lax.slice_in_dim(x, 0, count + 1, axis=axis)

    def upper(x):
        return lax.slice_in_dim(x, 1, count + 2, axis=axis)

    from_left = lower(right_face) - 0.5 * faces * (
        lower(slope) - (1.0 - 2.0 * faces / 3.0) * lower(curve)
    )
    from_right = upper(left_face) - 0.5 * faces * (
        upper(slope) + (1.0 + 2.0 * faces / 3.0) * upper(curve)
    )
    flux = faces * jnp.where(faces > 0, from_left, from_right)
    inner = piece(3, count + 3)
    return inner - (
        lax.slice_in_dim(flux, 1, count + 1, axis=axis)
        - lax.slice_in_dim(flux, 0, count, axis=axis)
    )


def lon_sweep(field, courant_x):
    count = field.shape[-1]
    padded = jnp.concatenate([field[..., -3:], field, field[..., :3]], axis=-1)
    faces = jnp.concatenate([courant_x[..., -1:], courant_x], axis=-1)
    return ppm_sweep(padded, faces, 3, count)


def lat_sweep(padded, faces, first_row, total_rows):
    count = padded.shape[2] - 6
    face_rows = first_row - 1 + jnp.arange(count + 1, dtype=jnp.int32)
    valid = ((face_rows >= 0) & (face_rows <= total_rows - 2)).astype(jnp.float32)
    faces = faces * valid[None, :, None]
    swept = ppm_sweep(padded, faces, 2, count)
    cell_rows = first_row + jnp.arange(count, dtype=jnp.int32)
    inside = ((cell_rows >= 0) & (cell_rows < total_rows)).astype(jnp.float32)
    return swept * inside[None, None, :, None]


def remap_columns(adv, thick, tg, levels_out):
    ks = jnp.arange(levels_out, dtype=jnp.int32)
    member = tg[None] == ks[:, None, None, None]
    mass = adv * thick[None]
    new_mass = jnp.sum(jnp.where(member[None], mass[:, None], 0.0), axis=2)
    new_thick = jnp.sum(jnp.where(member, thick[None], 0.0), axis=1)
    return jnp.transpose(new_mass / new_thick[None], (1, 0, 2, 3))


def local(tracers, courant_x, courant_y, thickness, targets):
    rows = tracers.shape[2]
    kinds = tracers.shape[0]
    total_rows = rows * lax.axis_size("lat")
    first_row = lax.axis_index("lat") * rows
    parts = lax.axis_size("lev")
    lon = tracers.shape[3]
    width = lon // parts
    levels_out = tracers.shape[1] * parts // 2
    field = tracers
    for step in range(SUBSTEPS):
        field = lon_sweep(field, courant_x)
        stacked = jnp.concatenate([field, courant_y[None]], axis=0)
        padded = padded_2(stacked, (("lat", 2),), 3)
        field = lat_sweep(padded[:kinds], padded[kinds][:, 2 : rows + 3], first_row, total_rows)
    blocks = jnp.transpose(field.reshape(field.shape[:3] + (parts, width)), (3, 0, 1, 2, 4))
    got = lax.all_to_all(blocks.reshape(parts, -1), "lev", split_axis=0, concat_axis=0, tiled=True).reshape(blocks.shape)
    adv = jnp.transpose(got, (1, 0, 2, 3, 4)).reshape(kinds, -1, rows, width)
    thick = jnp.transpose(thickness, (2, 0, 1))
    tg = jnp.transpose(targets, (2, 0, 1))
    out = remap_columns(adv, thick, tg, levels_out)
    back = lax.all_to_all(out.reshape(parts, -1), "lev", split_axis=0, concat_axis=0, tiled=True).reshape(out.shape)
    return jnp.transpose(back, (1, 2, 0, 3)).reshape(kinds, 1, rows, lon)


def solution(mesh):
    placed = (
        P(None, "lev", "lat", None),
        P("lev", "lat", None),
        P("lev", "lat", None),
        P("lat", "lev", None),
        P("lat", "lev", None),
    )
    return jax.shard_map(
        local, mesh=mesh, in_specs=placed, out_specs=P(None, "lev", "lat", None), check_vma=False
    )
```

```python
import jax
import jax.numpy as jnp
from jax import lax
from jax.sharding import PartitionSpec as P

SUBSTEPS = 2


def padded_2(cells, sides, width):
    for axis, dim in sides:
        count = lax.axis_size(axis)
        ends = count - 1
        head = lax.slice_in_dim(cells, 0, width, axis=dim)
        tail = lax.slice_in_dim(cells, cells.shape[dim] - width, cells.shape[dim], axis=dim)
        cells = jnp.concatenate(
            [
                lax.ppermute(tail, axis, [(i, (i + 1) % count) for i in range(ends)]),
                cells,
                lax.ppermute(head, axis, [((i + 1) % count, i) for i in range(ends)]),
            ],
            axis=dim,
        )
    return cells


def ppm_sweep(padded, faces, axis, count):

    def piece(start, stop):
        return lax.slice_in_dim(padded, start, stop, axis=axis)

    face_val = 7.0 / 12.0 * (piece(1, count + 4) + piece(2, count + 5)) - 1.0 / 12.0 * (
        piece(0, count + 3) + piece(3, count + 6)
    )
    cell_midpoint = piece(2, count + 4)
    left_face = lax.slice_in_dim(face_val, 0, count + 2, axis=axis)
    right_face = lax.slice_in_dim(face_val, 1, count + 3, axis=axis)
    slope = right_face - left_face
    curve = 6.0 * (cell_midpoint - 0.5 * (left_face + right_face))

    def lower(x):
        return lax.slice_in_dim(x, 0, count + 1, axis=axis)

    def upper(x):
        return lax.slice_in_dim(x, 1, count + 2, axis=axis)

    from_left = lower(right_face) - 0.5 * faces * (
        lower(slope) - (1.0 - 2.0 * faces / 3.0) * lower(curve)
    )
    from_right = upper(left_face) - 0.5 * faces * (
        upper(slope) + (1.0 + 2.0 * faces / 3.0) * upper(curve)
    )
    flux = faces * jnp.where(faces > 0, from_left, from_right)
    inner = piece(3, count + 3)
    return inner - (
        lax.slice_in_dim(flux, 1, count + 1, axis=axis)
        - lax.slice_in_dim(flux, 0, count, axis=axis)
    )


def lon_sweep(field, courant_x):
    count = field.shape[-1]
    padded = jnp.concatenate([field[..., -3:], field, field[..., :3]], axis=-1)
    faces = jnp.concatenate([courant_x[..., -1:], courant_x], axis=-1)
    return ppm_sweep(padded, faces, 3, count)


def lat_sweep(padded, faces, first_row, total_rows):
    count = padded.shape[2] - 6
    face_rows = first_row - 1 + jnp.arange(count + 1, dtype=jnp.int32)
    valid = ((face_rows >= 0) & (face_rows <= total_rows - 2)).astype(jnp.float32)
    faces = faces * valid[None, :, None]
    swept = ppm_sweep(padded, faces, 2, count)
    cell_rows = first_row + jnp.arange(count, dtype=jnp.int32)
    inside = ((cell_rows >= 0) & (cell_rows < total_rows)).astype(jnp.float32)
    return swept * inside[None, None, :, None]


def remap_columns(adv, thick, tg, levels_out):
    ks = jnp.arange(levels_out, dtype=jnp.int32)[:, None, None]
    mass = adv * thick[None]
    new_mass = 0.0
    new_thick = 0.0
    for shift in range(tg.shape[0] - levels_out + 1):
        member = tg[shift : shift + levels_out] == ks
        new_mass = new_mass + jnp.where(member[None], mass[:, shift : shift + levels_out], 0.0)
        new_thick = new_thick + jnp.where(member, thick[shift : shift + levels_out], 0.0)
    return jnp.transpose(new_mass / new_thick[None], (1, 0, 2, 3))


def local(tracers, courant_x, courant_y, thickness, targets):
    rows = tracers.shape[2]
    kinds = tracers.shape[0]
    total_rows = rows * lax.axis_size("lat")
    first_row = lax.axis_index("lat") * rows
    parts = lax.axis_size("lev")
    lon = tracers.shape[3]
    width = lon // parts
    levels_out = tracers.shape[1] * parts // 2
    field = tracers
    for step in range(SUBSTEPS):
        field = lon_sweep(field, courant_x)
        stacked = jnp.concatenate([field, courant_y[None]], axis=0)
        padded = padded_2(stacked, (("lat", 2),), 3)
        field = lat_sweep(padded[:kinds], padded[kinds][:, 2 : rows + 3], first_row, total_rows)
    blocks = jnp.transpose(field.reshape(field.shape[:3] + (parts, width)), (3, 0, 1, 2, 4))
    got = lax.all_to_all(blocks.reshape(parts, -1), "lev", split_axis=0, concat_axis=0, tiled=True).reshape(blocks.shape)
    adv = jnp.transpose(got, (1, 0, 2, 3, 4)).reshape(kinds, -1, rows, width)
    thick = jnp.transpose(thickness, (2, 0, 1))
    tg = jnp.transpose(targets, (2, 0, 1))
    out = remap_columns(adv, thick, tg, levels_out)
    back = lax.all_to_all(out.reshape(parts, -1), "lev", split_axis=0, concat_axis=0, tiled=True).reshape(out.shape)
    return jnp.transpose(back, (1, 2, 0, 3)).reshape(kinds, 1, rows, lon)


def solution(mesh):
    placed = (
        P(None, "lev", "lat", None),
        P("lev", "lat", None),
        P("lev", "lat", None),
        P("lat", "lev", None),
        P("lat", "lev", None),
    )
    return jax.shard_map(
        local, mesh=mesh, in_specs=placed, out_specs=P(None, "lev", "lat", None), check_vma=False
    )
```

```python
import jax
import jax.numpy as jnp
from jax import lax
from jax.sharding import PartitionSpec as P

SUBSTEPS = 2


def padded_2(cells, sides, width):
    for axis, dim in sides:
        count = lax.axis_size(axis)
        ends = count - 1
        head = lax.slice_in_dim(cells, 0, width, axis=dim)
        tail = lax.slice_in_dim(cells, cells.shape[dim] - width, cells.shape[dim], axis=dim)
        cells = jnp.concatenate(
            [
                lax.ppermute(tail, axis, [(i, (i + 1) % count) for i in range(ends)]),
                cells,
                lax.ppermute(head, axis, [((i + 1) % count, i) for i in range(ends)]),
            ],
            axis=dim,
        )
    return cells


def ppm_sweep(padded, faces, axis, count):

    def piece(start, stop):
        return lax.slice_in_dim(padded, start, stop, axis=axis)

    face_val = 7.0 / 12.0 * (piece(1, count + 4) + piece(2, count + 5)) - 1.0 / 12.0 * (
        piece(0, count + 3) + piece(3, count + 6)
    )
    cell_midpoint = piece(2, count + 4)
    left_face = lax.slice_in_dim(face_val, 0, count + 2, axis=axis)
    right_face = lax.slice_in_dim(face_val, 1, count + 3, axis=axis)
    slope = right_face - left_face
    curve = 6.0 * (cell_midpoint - 0.5 * (left_face + right_face))

    def lower(x):
        return lax.slice_in_dim(x, 0, count + 1, axis=axis)

    def upper(x):
        return lax.slice_in_dim(x, 1, count + 2, axis=axis)

    from_left = lower(right_face) - 0.5 * faces * (
        lower(slope) - (1.0 - 2.0 * faces / 3.0) * lower(curve)
    )
    from_right = upper(left_face) - 0.5 * faces * (
        upper(slope) + (1.0 + 2.0 * faces / 3.0) * upper(curve)
    )
    flux = faces * jnp.where(faces > 0, from_left, from_right)
    inner = piece(3, count + 3)
    return inner - (
        lax.slice_in_dim(flux, 1, count + 1, axis=axis)
        - lax.slice_in_dim(flux, 0, count, axis=axis)
    )


def lon_sweep(field, courant_x):
    count = field.shape[-1]
    padded = jnp.concatenate([field[..., -3:], field, field[..., :3]], axis=-1)
    faces = jnp.concatenate([courant_x[..., -1:], courant_x], axis=-1)
    return ppm_sweep(padded, faces, 3, count)


def lat_sweep(padded, faces, first_row, total_rows):
    count = padded.shape[2] - 6
    face_rows = first_row - 1 + jnp.arange(count + 1, dtype=jnp.int32)
    valid = ((face_rows >= 0) & (face_rows <= total_rows - 2)).astype(jnp.float32)
    faces = faces * valid[None, :, None]
    swept = ppm_sweep(padded, faces, 2, count)
    cell_rows = first_row + jnp.arange(count, dtype=jnp.int32)
    inside = ((cell_rows >= 0) & (cell_rows < total_rows)).astype(jnp.float32)
    return swept * inside[None, None, :, None]


def remap_columns(adv, thick, tg, levels_out):
    ks = jnp.arange(levels_out, dtype=jnp.int32)[:, None, None]
    mass = adv * thick[None]
    new_mass = 0.0
    new_thick = 0.0
    for shift in range(tg.shape[0] - levels_out + 1):
        member = tg[shift : shift + levels_out] == ks
        new_mass = new_mass + jnp.where(member[None], mass[:, shift : shift + levels_out], 0.0)
        new_thick = new_thick + jnp.where(member, thick[shift : shift + levels_out], 0.0)
    return jnp.transpose(new_mass / new_thick[None], (1, 0, 2, 3))


def local(tracers, courant_x, courant_y, thickness, targets):
    rows = tracers.shape[2]
    kinds = tracers.shape[0]
    total_rows = rows * lax.axis_size("lat")
    first_row = lax.axis_index("lat") * rows
    parts = lax.axis_size("lev")
    lon = tracers.shape[3]
    width = lon // parts
    levels_out = tracers.shape[1] * parts // 2
    field = tracers
    faces_y = None
    for step in range(SUBSTEPS):
        field = lon_sweep(field, courant_x)
        if faces_y is None:
            padded = padded_2(jnp.concatenate([field, courant_y[None]], axis=0), (("lat", 2),), 3)
            faces_y = padded[kinds][:, 2 : rows + 3]
        else:
            padded = padded_2(field, (("lat", 2),), 3)
        field = lat_sweep(padded[:kinds], faces_y, first_row, total_rows)
    blocks = jnp.transpose(field.reshape(field.shape[:3] + (parts, width)), (3, 0, 1, 2, 4))
    got = lax.all_to_all(blocks.reshape(parts, -1), "lev", split_axis=0, concat_axis=0, tiled=True).reshape(blocks.shape)
    adv = jnp.transpose(got, (1, 0, 2, 3, 4)).reshape(kinds, -1, rows, width)
    thick = jnp.transpose(thickness, (2, 0, 1))
    tg = jnp.transpose(targets, (2, 0, 1))
    out = remap_columns(adv, thick, tg, levels_out)
    back = lax.all_to_all(out.reshape(parts, -1), "lev", split_axis=0, concat_axis=0, tiled=True).reshape(out.shape)
    return jnp.transpose(back, (1, 2, 0, 3)).reshape(kinds, 1, rows, lon)


def solution(mesh):
    placed = (
        P(None, "lev", "lat", None),
        P("lev", "lat", None),
        P("lev", "lat", None),
        P("lat", "lev", None),
        P("lat", "lev", None),
    )
    return jax.shard_map(
        local, mesh=mesh, in_specs=placed, out_specs=P(None, "lev", "lat", None), check_vma=False
    )
```

```python
import jax
import jax.numpy as jnp
from jax import lax
from jax.sharding import PartitionSpec as P

SUBSTEPS = 2


def padded_2(cells, sides, width):
    for axis, dim in sides:
        count = lax.axis_size(axis)
        ends = count - 1
        head = lax.slice_in_dim(cells, 0, width, axis=dim)
        tail = lax.slice_in_dim(cells, cells.shape[dim] - width, cells.shape[dim], axis=dim)
        cells = jnp.concatenate(
            [
                lax.ppermute(tail, axis, [(i, (i + 1) % count) for i in range(ends)]),
                cells,
                lax.ppermute(head, axis, [((i + 1) % count, i) for i in range(ends)]),
            ],
            axis=dim,
        )
    return cells


def ppm_sweep(padded, faces, axis, count):

    def piece(start, stop):
        return lax.slice_in_dim(padded, start, stop, axis=axis)

    face_val = 7.0 / 12.0 * (piece(1, count + 4) + piece(2, count + 5)) - 1.0 / 12.0 * (
        piece(0, count + 3) + piece(3, count + 6)
    )
    cell_midpoint = piece(2, count + 4)
    left_face = lax.slice_in_dim(face_val, 0, count + 2, axis=axis)
    right_face = lax.slice_in_dim(face_val, 1, count + 3, axis=axis)
    slope = right_face - left_face
    curve = 6.0 * (cell_midpoint - 0.5 * (left_face + right_face))

    def lower(x):
        return lax.slice_in_dim(x, 0, count + 1, axis=axis)

    def upper(x):
        return lax.slice_in_dim(x, 1, count + 2, axis=axis)

    from_left = lower(right_face) - 0.5 * faces * (
        lower(slope) - (1.0 - 2.0 * faces / 3.0) * lower(curve)
    )
    from_right = upper(left_face) - 0.5 * faces * (
        upper(slope) + (1.0 + 2.0 * faces / 3.0) * upper(curve)
    )
    flux = faces * jnp.where(faces > 0, from_left, from_right)
    inner = piece(3, count + 3)
    return inner - (
        lax.slice_in_dim(flux, 1, count + 1, axis=axis)
        - lax.slice_in_dim(flux, 0, count, axis=axis)
    )


def lon_sweep(field, courant_x):
    count = field.shape[-1]
    padded = jnp.concatenate([field[..., -3:], field, field[..., :3]], axis=-1)
    faces = jnp.concatenate([courant_x[..., -1:], courant_x], axis=-1)
    return ppm_sweep(padded, faces, 3, count)


def lat_sweep(padded, faces, first_row, total_rows):
    count = padded.shape[2] - 6
    face_rows = first_row - 1 + jnp.arange(count + 1, dtype=jnp.int32)
    valid = ((face_rows >= 0) & (face_rows <= total_rows - 2)).astype(jnp.float32)
    faces = faces * valid[None, :, None]
    swept = ppm_sweep(padded, faces, 2, count)
    cell_rows = first_row + jnp.arange(count, dtype=jnp.int32)
    inside = ((cell_rows >= 0) & (cell_rows < total_rows)).astype(jnp.float32)
    return swept * inside[None, None, :, None]


def remap_columns(adv, thick, tg, levels_out):
    ks = jnp.arange(levels_out, dtype=jnp.int32)[:, None, None]
    mass = adv * thick[None]
    new_mass = 0.0
    new_thick = 0.0
    for shift in range(tg.shape[0] - levels_out + 1):
        member = tg[shift : shift + levels_out] == ks
        new_mass = new_mass + jnp.where(member[None], mass[:, shift : shift + levels_out], 0.0)
        new_thick = new_thick + jnp.where(member, thick[shift : shift + levels_out], 0.0)
    return jnp.transpose(new_mass / new_thick[None], (1, 0, 2, 3))


def local(tracers, courant_x, courant_y, thickness, targets):
    rows = tracers.shape[2]
    kinds = tracers.shape[0]
    total_rows = rows * lax.axis_size("lat")
    first_row = lax.axis_index("lat") * rows
    parts = lax.axis_size("lev")
    lon = tracers.shape[3]
    width = lon // parts
    levels_out = tracers.shape[1] * parts // 2
    field = tracers
    faces_y = None
    for step in range(SUBSTEPS):
        field = lon_sweep(field, courant_x)
        if faces_y is None:
            count = lax.axis_size("lat")
            stacked = jnp.concatenate([field, courant_y[None]], axis=0)
            south = lax.ppermute(stacked[:, :, rows - 3 :], "lat", [(i, i + 1) for i in range(count - 1)])
            north = lax.ppermute(field[:, :, :3], "lat", [(i + 1, i) for i in range(count - 1)])
            padded = jnp.concatenate([south[:kinds], field, north], axis=2)
            faces_y = jnp.concatenate([south[kinds], courant_y], axis=1)[:, 2 : rows + 3]
        else:
            padded = padded_2(field, (("lat", 2),), 3)
        field = lat_sweep(padded[:kinds], faces_y, first_row, total_rows)
    blocks = jnp.transpose(field.reshape(field.shape[:3] + (parts, width)), (3, 0, 1, 2, 4))
    got = lax.all_to_all(blocks.reshape(parts, -1), "lev", split_axis=0, concat_axis=0, tiled=True).reshape(blocks.shape)
    adv = jnp.transpose(got, (1, 0, 2, 3, 4)).reshape(kinds, -1, rows, width)
    thick = jnp.transpose(thickness, (2, 0, 1))
    tg = jnp.transpose(targets, (2, 0, 1))
    out = remap_columns(adv, thick, tg, levels_out)
    back = lax.all_to_all(out.reshape(parts, -1), "lev", split_axis=0, concat_axis=0, tiled=True).reshape(out.shape)
    return jnp.transpose(back, (1, 2, 0, 3)).reshape(kinds, 1, rows, lon)


def solution(mesh):
    placed = (
        P(None, "lev", "lat", None),
        P("lev", "lat", None),
        P("lev", "lat", None),
        P("lat", "lev", None),
        P("lat", "lev", None),
    )
    return jax.shard_map(
        local, mesh=mesh, in_specs=placed, out_specs=P(None, "lev", "lat", None), check_vma=False
    )
```

```python
import jax
import jax.numpy as jnp
from jax import lax
from jax.sharding import PartitionSpec as P

SUBSTEPS = 2


def padded_2(cells, sides, width):
    for axis, dim in sides:
        count = lax.axis_size(axis)
        ends = count - 1
        head = lax.slice_in_dim(cells, 0, width, axis=dim)
        tail = lax.slice_in_dim(cells, cells.shape[dim] - width, cells.shape[dim], axis=dim)
        cells = jnp.concatenate(
            [
                lax.ppermute(tail, axis, [(i, (i + 1) % count) for i in range(ends)]),
                cells,
                lax.ppermute(head, axis, [((i + 1) % count, i) for i in range(ends)]),
            ],
            axis=dim,
        )
    return cells


def ppm_sweep(padded, faces, axis, count):

    def piece(start, stop):
        return lax.slice_in_dim(padded, start, stop, axis=axis)

    face_val = 7.0 / 12.0 * (piece(1, count + 4) + piece(2, count + 5)) - 1.0 / 12.0 * (
        piece(0, count + 3) + piece(3, count + 6)
    )
    cell_midpoint = piece(2, count + 4)
    left_face = lax.slice_in_dim(face_val, 0, count + 2, axis=axis)
    right_face = lax.slice_in_dim(face_val, 1, count + 3, axis=axis)
    slope = right_face - left_face
    curve = 6.0 * (cell_midpoint - 0.5 * (left_face + right_face))

    def lower(x):
        return lax.slice_in_dim(x, 0, count + 1, axis=axis)

    def upper(x):
        return lax.slice_in_dim(x, 1, count + 2, axis=axis)

    from_left = lower(right_face) - 0.5 * faces * (
        lower(slope) - (1.0 - 2.0 * faces / 3.0) * lower(curve)
    )
    from_right = upper(left_face) - 0.5 * faces * (
        upper(slope) + (1.0 + 2.0 * faces / 3.0) * upper(curve)
    )
    flux = faces * jnp.where(faces > 0, from_left, from_right)
    inner = piece(3, count + 3)
    return inner - (
        lax.slice_in_dim(flux, 1, count + 1, axis=axis)
        - lax.slice_in_dim(flux, 0, count, axis=axis)
    )


def lon_sweep(field, courant_x):
    count = field.shape[-1]
    padded = jnp.concatenate([field[..., -3:], field, field[..., :3]], axis=-1)
    faces = jnp.concatenate([courant_x[..., -1:], courant_x], axis=-1)
    return ppm_sweep(padded, faces, 3, count)


def lat_sweep(padded, faces, first_row, total_rows):
    count = padded.shape[2] - 6
    face_rows = first_row - 1 + jnp.arange(count + 1, dtype=jnp.int32)
    valid = ((face_rows >= 0) & (face_rows <= total_rows - 2)).astype(jnp.float32)
    faces = faces * valid[None, :, None]
    swept = ppm_sweep(padded, faces, 2, count)
    cell_rows = first_row + jnp.arange(count, dtype=jnp.int32)
    inside = ((cell_rows >= 0) & (cell_rows < total_rows)).astype(jnp.float32)
    return swept * inside[None, None, :, None]


def remap_columns(adv, thick, tg, levels_out):
    ks = jnp.arange(levels_out, dtype=jnp.int32)[:, None, None]
    mass = adv * thick[None]
    new_mass = 0.0
    new_thick = 0.0
    for shift in range(tg.shape[0] - levels_out + 1):
        member = tg[shift : shift + levels_out] == ks
        new_mass = new_mass + jnp.where(member[None], mass[:, shift : shift + levels_out], 0.0)
        new_thick = new_thick + jnp.where(member, thick[shift : shift + levels_out], 0.0)
    return jnp.transpose(new_mass / new_thick[None], (1, 0, 2, 3))


def local(tracers, courant_x, courant_y, thickness, targets):
    rows = tracers.shape[2]
    kinds = tracers.shape[0]
    total_rows = rows * lax.axis_size("lat")
    first_row = lax.axis_index("lat") * rows
    parts = lax.axis_size("lev")
    lon = tracers.shape[3]
    width = lon // parts
    levels_out = tracers.shape[1] * parts // 2
    field = tracers
    faces_y = None
    for step in range(SUBSTEPS):
        before = field
        field = lon_sweep(field, courant_x)
        if faces_y is None:
            count = lax.axis_size("lat")
            stacked = jnp.concatenate([field, courant_y[None]], axis=0)
            south = lax.ppermute(stacked[:, :, rows - 3 :], "lat", [(i, i + 1) for i in range(count - 1)])
            north = lax.ppermute(field[:, :, :3], "lat", [(i + 1, i) for i in range(count - 1)])
            padded = jnp.concatenate([south[:kinds], field, north], axis=2)
            faces_y = jnp.concatenate([south[kinds], courant_y], axis=1)[:, 2 : rows + 3]
        else:
            count = lax.axis_size("lat")
            south = lax.ppermute(
                lon_sweep(before[:, :, rows - 3 :], courant_x[:, rows - 3 :]),
                "lat",
                [(i, i + 1) for i in range(count - 1)],
            )
            north = lax.ppermute(
                lon_sweep(before[:, :, :3], courant_x[:, :3]), "lat", [(i + 1, i) for i in range(count - 1)]
            )
            padded = jnp.concatenate([south, field, north], axis=2)
        field = lat_sweep(padded[:kinds], faces_y, first_row, total_rows)
    blocks = jnp.transpose(field.reshape(field.shape[:3] + (parts, width)), (3, 0, 1, 2, 4))
    got = lax.all_to_all(blocks.reshape(parts, -1), "lev", split_axis=0, concat_axis=0, tiled=True).reshape(blocks.shape)
    adv = jnp.transpose(got, (1, 0, 2, 3, 4)).reshape(kinds, -1, rows, width)
    thick = jnp.transpose(thickness, (2, 0, 1))
    tg = jnp.transpose(targets, (2, 0, 1))
    out = remap_columns(adv, thick, tg, levels_out)
    back = lax.all_to_all(out.reshape(parts, -1), "lev", split_axis=0, concat_axis=0, tiled=True).reshape(out.shape)
    return jnp.transpose(back, (1, 2, 0, 3)).reshape(kinds, 1, rows, lon)


def solution(mesh):
    placed = (
        P(None, "lev", "lat", None),
        P("lev", "lat", None),
        P("lev", "lat", None),
        P("lat", "lev", None),
        P("lat", "lev", None),
    )
    return jax.shard_map(
        local, mesh=mesh, in_specs=placed, out_specs=P(None, "lev", "lat", None), check_vma=False
    )
```

```python
import jax
import jax.numpy as jnp
from jax import lax
from jax.sharding import PartitionSpec as P

SUBSTEPS = 2


def padded_2(cells, sides, width):
    for axis, dim in sides:
        count = lax.axis_size(axis)
        ends = count - 1
        head = lax.slice_in_dim(cells, 0, width, axis=dim)
        tail = lax.slice_in_dim(cells, cells.shape[dim] - width, cells.shape[dim], axis=dim)
        cells = jnp.concatenate(
            [
                lax.ppermute(tail, axis, [(i, (i + 1) % count) for i in range(ends)]),
                cells,
                lax.ppermute(head, axis, [((i + 1) % count, i) for i in range(ends)]),
            ],
            axis=dim,
        )
    return cells


def ppm_sweep(padded, faces, axis, count):

    def piece(start, stop):
        return lax.slice_in_dim(padded, start, stop, axis=axis)

    face_val = 7.0 / 12.0 * (piece(1, count + 4) + piece(2, count + 5)) - 1.0 / 12.0 * (
        piece(0, count + 3) + piece(3, count + 6)
    )
    cell_midpoint = piece(2, count + 4)
    left_face = lax.slice_in_dim(face_val, 0, count + 2, axis=axis)
    right_face = lax.slice_in_dim(face_val, 1, count + 3, axis=axis)
    slope = right_face - left_face
    curve = 6.0 * (cell_midpoint - 0.5 * (left_face + right_face))

    def lower(x):
        return lax.slice_in_dim(x, 0, count + 1, axis=axis)

    def upper(x):
        return lax.slice_in_dim(x, 1, count + 2, axis=axis)

    from_left = lower(right_face) - 0.5 * faces * (
        lower(slope) - (1.0 - 2.0 * faces / 3.0) * lower(curve)
    )
    from_right = upper(left_face) - 0.5 * faces * (
        upper(slope) + (1.0 + 2.0 * faces / 3.0) * upper(curve)
    )
    flux = faces * jnp.where(faces > 0, from_left, from_right)
    inner = piece(3, count + 3)
    return inner - (
        lax.slice_in_dim(flux, 1, count + 1, axis=axis)
        - lax.slice_in_dim(flux, 0, count, axis=axis)
    )


def lon_sweep(field, courant_x):
    count = field.shape[-1]
    padded = jnp.concatenate([field[..., -3:], field, field[..., :3]], axis=-1)
    faces = jnp.concatenate([courant_x[..., -1:], courant_x], axis=-1)
    faces = lax.optimization_barrier(faces)
    return ppm_sweep(padded, faces, 3, count)


def lat_sweep(padded, faces, first_row, total_rows):
    count = padded.shape[2] - 6
    face_rows = first_row - 1 + jnp.arange(count + 1, dtype=jnp.int32)
    valid = ((face_rows >= 0) & (face_rows <= total_rows - 2)).astype(jnp.float32)
    faces = faces * valid[None, :, None]
    swept = ppm_sweep(padded, faces, 2, count)
    cell_rows = first_row + jnp.arange(count, dtype=jnp.int32)
    inside = ((cell_rows >= 0) & (cell_rows < total_rows)).astype(jnp.float32)
    return swept * inside[None, None, :, None]


def remap_columns(adv, thick, tg, levels_out):
    ks = jnp.arange(levels_out, dtype=jnp.int32)[:, None, None]
    mass = adv * thick[None]
    new_mass = 0.0
    new_thick = 0.0
    for shift in range(tg.shape[0] - levels_out + 1):
        member = tg[shift : shift + levels_out] == ks
        new_mass = new_mass + jnp.where(member[None], mass[:, shift : shift + levels_out], 0.0)
        new_thick = new_thick + jnp.where(member, thick[shift : shift + levels_out], 0.0)
    return jnp.transpose(new_mass / new_thick[None], (1, 0, 2, 3))


def local(tracers, courant_x, courant_y, thickness, targets):
    rows = tracers.shape[2]
    kinds = tracers.shape[0]
    total_rows = rows * lax.axis_size("lat")
    first_row = lax.axis_index("lat") * rows
    parts = lax.axis_size("lev")
    lon = tracers.shape[3]
    width = lon // parts
    levels_out = tracers.shape[1] * parts // 2
    field = tracers
    faces_y = None
    for step in range(SUBSTEPS):
        field = lon_sweep(field, courant_x)
        if faces_y is None:
            count = lax.axis_size("lat")
            stacked = jnp.concatenate([field, courant_y[None]], axis=0)
            south = lax.ppermute(stacked[:, :, rows - 3 :], "lat", [(i, i + 1) for i in range(count - 1)])
            north = lax.ppermute(field[:, :, :3], "lat", [(i + 1, i) for i in range(count - 1)])
            padded = jnp.concatenate([south[:kinds], field, north], axis=2)
            faces_y = jnp.concatenate([south[kinds], courant_y], axis=1)[:, 2 : rows + 3]
        else:
            padded = padded_2(field, (("lat", 2),), 3)
        field = lat_sweep(padded[:kinds], faces_y, first_row, total_rows)
    blocks = jnp.transpose(field.reshape(field.shape[:3] + (parts, width)), (3, 0, 1, 2, 4))
    got = lax.all_to_all(blocks.reshape(parts, -1), "lev", split_axis=0, concat_axis=0, tiled=True).reshape(blocks.shape)
    adv = jnp.transpose(got, (1, 0, 2, 3, 4)).reshape(kinds, -1, rows, width)
    thick = jnp.transpose(thickness, (2, 0, 1))
    tg = jnp.transpose(targets, (2, 0, 1))
    out = remap_columns(adv, thick, tg, levels_out)
    back = lax.all_to_all(out.reshape(parts, -1), "lev", split_axis=0, concat_axis=0, tiled=True).reshape(out.shape)
    return jnp.transpose(back, (1, 2, 0, 3)).reshape(kinds, 1, rows, lon)


def solution(mesh):
    placed = (
        P(None, "lev", "lat", None),
        P("lev", "lat", None),
        P("lev", "lat", None),
        P("lat", "lev", None),
        P("lat", "lev", None),
    )
    return jax.shard_map(
        local, mesh=mesh, in_specs=placed, out_specs=P(None, "lev", "lat", None), check_vma=False
    )
```
